128 devices in a mesh: blk: 16 (over z_lo, y, core), group: 8 (over x, z_hi).
Axes of the slice: x: 4, y: 4, z: 4 (z_hi: 2, z_lo: 2; z = z_hi * 2 + z_lo), core: 2. Of those that a mesh axis runs over, the one named last changes fastest.
Arguments:
- centres: bfloat16 [262144, 1024], P(('blk', 'group')), may hold values from -8 to 8
- batch_x: bfloat16 [2048, 1024], P(('blk', 'group')), may hold values from -8 to 8
- grad: bfloat16 [2048, 1000], P(('blk', 'group')), may hold values from -0.29882812 to 0.29882812
- eigvec: float32 [65536, 128], P(('blk', 'group')), may hold values from -0.0234375 to 0.0234375
- eig_scale: float32 [128], replicated, may hold values from 2 to 20
- sub_index: int32 [65536], P(('blk', 'group')), may hold values from 0 to 262143, as said below
Outputs:
- update: float32 [262144, 1000], P(('blk', 'group'))
The draws below stay inside these ranges and needn't reach their ends.
Inputs may be any that keep to these rules, and one draw needn't show every extreme that they name: `sub_index`: all entries are distinct. Entry i of the block of 512 entries that device index k of blk+group holds names a centre among rows (k // 8) * 8 * 2048 to (k // 8 + 1) * 8 * 2048 - 1; among one such block at most 128 entries name rows of any one aligned run of 2048 centres, and every block has exactly 128 in one run.
All inputs are finite; a program needn't handle non-finite values.
Results may differ from the reference program's by a relative error of at most 0.0027.
Values may be sent and summed in bfloat16 or wider, within the bound.
No kernel may reach another device: no remote copies, remote signals or barrier semaphores. Data moves between devices by JAX's collectives and lax.ppermute only.
A program may use at most 128 MiB of HBM per device.

```python
import math
import jax
import jax.numpy as jnp
from jax import lax

D = 1024
CLS = 1000
Q = 128
C_DEV = 2048
NYS_DEV = 512
CAP = 128
CENT = 262144
BATCH = 2048
NYS = 65536
CLUST = 256
N_BLK = 16
N_GROUP = 8


def cluster_points(key, count, salt):
    means_key = jax.random.fold_in(key, 101)
    means = 1.5 * jax.random.truncated_normal(means_key, -4.0, 4.0, (CLUST, D), jnp.float32)
    labels = jax.random.randint(jax.random.fold_in(key, salt), (count,), 0, CLUST)
    noise_key = jax.random.fold_in(key, salt + 1)
    noise = 0.4 * jax.random.truncated_normal(noise_key, -4.0, 4.0, (count, D), jnp.float32)
    return (means[labels] + noise).astype(jnp.bfloat16)


def draw_centres(key, part):
    return cluster_points(key, CENT, 202)


def draw_batch_x(key, part):
    return cluster_points(key, BATCH, 303)


def draw_sub_index(key, part):
    count = N_BLK * N_GROUP
    perm_keys = jax.random.split(jax.random.fold_in(key, 11), count)
    perm_table = jax.vmap(lambda k: jax.random.permutation(k, C_DEV))(perm_keys)
    owner_keys = jax.random.split(jax.random.fold_in(key, 23), count)

    def owner_rows(okey, device):
        key_first, key_pool, key_order = jax.random.split(okey, 3)
        first = jax.random.randint(key_first, (), 0, N_GROUP)
        pool = 1 + jnp.arange((N_GROUP - 1) * CAP, dtype=jnp.int32) // CAP
        pool = jax.random.permutation(key_pool, pool)[:NYS_DEV - CAP]
        offsets = jnp.concatenate([jnp.zeros((CAP,), jnp.int32), pool])
        offsets = jax.random.permutation(key_order, offsets)
        holder = (first + offsets) % N_GROUP
        onehot = (holder[:, None] == jnp.arange(N_GROUP, dtype=jnp.int32)[None, :]).astype(jnp.int32)
        order_in = jnp.sum(jnp.cumsum(onehot, axis=0) * onehot, axis=1) - 1
        slab = device // N_GROUP
        member = device % N_GROUP
        target = slab * N_GROUP + holder
        local_row = perm_table[target, member * CAP + order_in]
        return (target * C_DEV + local_row).astype(jnp.int32)
    devices = jnp.arange(count, dtype=jnp.int32)
    return jax.vmap(owner_rows)(owner_keys, devices).reshape(-1)


def block_levels(stream_key, shape, shards, low, high):
    level = 1.0
    for position, blocks in shards:
        steps = jax.random.uniform(jax.random.fold_in(jax.random.fold_in(stream_key, 6), position), (blocks,), jnp.float32, low / len(shards), high / len(shards))
        level = level * jnp.repeat(jnp.exp(steps), shape[position] // blocks).reshape((-1,) + (1,) * (len(shape) - 1 - position))
    return level


def gaussian(rng, dims, width, most, shards=(), kind=jnp.bfloat16):
    array = jax.random.normal(rng, dims, jnp.float32) * width
    if len(shards) > 0:
        array = block_levels(rng, dims, shards, -0.22, 0.18) * array
    return jnp.clip(array, min=-most, max=most).astype(kind)


def setup_inputs(seed: int = 0) -> dict:
    key_of = jax.random.split(jax.random.key(seed), 7)
    centres = draw_centres(jax.random.fold_in(key_of[6], 71), 0)
    batch_x = draw_batch_x(jax.random.fold_in(key_of[6], 71), 0)
    grad = gaussian(key_of[2], (BATCH, CLS), 0.05, 0.29882812, ((0, 128),))
    eigvec = gaussian(key_of[3], (NYS, Q), NYS ** -0.5, 0.0234375, ((0, 128),), jnp.float32)
    eig_scale = jnp.clip(jnp.exp(jax.random.uniform(key_of[4], (Q,), jnp.float32, math.log(2.0), math.log(20.0))), 2.0, 20.0)
    sub_index = draw_sub_index(jax.random.fold_in(key_of[6], 71), 0)
    return {"centres": centres, "batch_x": batch_x, "grad": grad, "eigvec": eigvec, "eig_scale": eig_scale, "sub_index": sub_index}


def reference(centres, batch_x, grad, eigvec, eig_scale, sub_index):
    batch_sq = jnp.sum(jnp.square(batch_x.astype(jnp.float32)), axis=1)

    def centre_block(block_rows):
        centre_sq = jnp.sum(jnp.square(block_rows.astype(jnp.float32)), axis=1)
        inner_prod = jnp.dot(block_rows, batch_x.T, preferred_element_type=jnp.float32)
        distance = centre_sq[:, None] + batch_sq[None, :] - 2.0 * inner_prod
        kernel_tile = jnp.exp(-distance / (2.0 * D)).astype(jnp.bfloat16)
        return jnp.dot(kernel_tile, grad, preferred_element_type=jnp.float32)

    kernel_grad = lax.map(centre_block, centres.reshape(CENT // C_DEV, C_DEV, D)).reshape(CENT, CLS)
    picked = kernel_grad[sub_index]
    projected = jnp.dot(eigvec.T, picked, precision=lax.Precision.HIGHEST)
    correction = jnp.dot(eigvec * eig_scale[None, :], projected, precision=lax.Precision.HIGHEST)
    return kernel_grad.at[sub_index].add(-correction)
```

```python
import jax
import jax.numpy as jnp
from jax import lax
from jax.sharding import PartitionSpec as P

D = 1024
CAP = 128


def body(centres, batch_x, grad, eigvec, eig_scale, sub_index):
    dims = batch_x.shape[1]
    centre_sq = jnp.sum(jnp.square(centres.astype(jnp.float32)), axis=1)
    joined = jnp.concatenate([batch_x, grad], axis=1)
    joined = lax.all_gather(joined, "group", axis=0, tiled=True)
    joined = lax.all_gather(joined, "blk", axis=0, tiled=True)
    piece_x = joined[:, :dims]
    piece_g = joined[:, dims:]
    batch_sq = jnp.sum(jnp.square(piece_x.astype(jnp.float32)), axis=1)
    inner_prod = jnp.einsum("cd,bd->cb", centres, piece_x, preferred_element_type=jnp.float32)
    distance = centre_sq[:, None] + batch_sq[None, :] - 2.0 * inner_prod
    kernel_tile = jnp.exp(-distance / (2.0 * D)).astype(jnp.bfloat16)
    kernel_grad = jnp.dot(kernel_tile, piece_g, preferred_element_type=jnp.float32)
    groups = lax.axis_size("group")
    rows_each = centres.shape[0]
    holder = sub_index // rows_each % groups
    local_row = sub_index % rows_each
    onehot = (holder[:, None] == jnp.arange(groups, dtype=jnp.int32)[None, :]).astype(jnp.int32)
    order_in = jnp.sum(jnp.cumsum(onehot, axis=0) * onehot, axis=1) - 1
    position = holder * CAP + order_in
    slot_table = jnp.zeros((groups * CAP,), jnp.int32).at[position].set(local_row)
    eig_table = jnp.zeros((groups * CAP, eigvec.shape[1]), jnp.float32).at[position].set(eigvec)
    got_slots = lax.all_to_all(slot_table, "group", split_axis=0, concat_axis=0, tiled=True)
    got_eig = lax.all_to_all(eig_table, "group", split_axis=0, concat_axis=0, tiled=True)
    picked = kernel_grad[got_slots]
    projected = lax.psum(
        jnp.einsum("sq,sk->qk", got_eig, picked, precision=lax.Precision.HIGHEST), ("blk", "group")
    )
    correction = jnp.dot(got_eig * eig_scale[None, :], projected, precision=lax.Precision.HIGHEST)
    return kernel_grad.at[got_slots].add(-correction)


def solution(mesh):
    in_specs = (
        P(("blk", "group"), None),
        P(("blk", "group"), None),
        P(("blk", "group"), None),
        P(("blk", "group"), None),
        P(),
        P(("blk", "group")),
    )
    out_specs = P(("blk", "group"), None)
    return jax.shard_map(body, mesh=mesh, in_specs=in_specs, out_specs=out_specs, check_vma=False)
```

```python
import jax
import jax.numpy as jnp
from jax import lax
from jax.sharding import PartitionSpec as P

D = 1024
CAP = 128


SUM_BITS = (3, 6, 1, 4, 0, 2, 5)


def tree_psum(value, axes):
    size = lax.axis_size(axes)
    me = lax.axis_index(axes)
    bits = [b for b in SUM_BITS if (1 << b) < size]
    current = value
    for b in bits:
        pairs = [(k, k ^ (1 << b)) for k in range(size)]
        half = current.shape[0] // 2
        upper = (me >> b) & 1
        keep = lax.dynamic_slice_in_dim(current, upper * half, half, axis=0)
        send = lax.dynamic_slice_in_dim(current, (1 - upper) * half, half, axis=0)
        current = keep + lax.ppermute(send, axes, pairs)
    for b in reversed(bits):
        pairs = [(k, k ^ (1 << b)) for k in range(size)]
        upper = (me >> b) & 1
        other = lax.ppermute(current, axes, pairs)
        current = jnp.where(
            upper == 0, jnp.concatenate([current, other]), jnp.concatenate([other, current])
        )
    return current


def body(centres, batch_x, grad, eigvec, eig_scale, sub_index):
    dims = batch_x.shape[1]
    centre_sq = jnp.sum(jnp.square(centres.astype(jnp.float32)), axis=1)
    joined = jnp.concatenate([batch_x, grad], axis=1)
    joined = lax.all_gather(joined, "group", axis=0, tiled=True)
    joined = lax.all_gather(joined, "blk", axis=0, tiled=True)
    piece_x = joined[:, :dims]
    piece_g = joined[:, dims:]
    batch_sq = jnp.sum(jnp.square(piece_x.astype(jnp.float32)), axis=1)
    inner_prod = jnp.einsum("cd,bd->cb", centres, piece_x, preferred_element_type=jnp.float32)
    distance = centre_sq[:, None] + batch_sq[None, :] - 2.0 * inner_prod
    kernel_tile = jnp.exp(-distance / (2.0 * D)).astype(jnp.bfloat16)
    kernel_grad = jnp.dot(kernel_tile, piece_g, preferred_element_type=jnp.float32)
    groups = lax.axis_size("group")
    rows_each = centres.shape[0]
    holder = sub_index // rows_each % groups
    local_row = sub_index % rows_each
    onehot = (holder[:, None] == jnp.arange(groups, dtype=jnp.int32)[None, :]).astype(jnp.int32)
    order_in = jnp.sum(jnp.cumsum(onehot, axis=0) * onehot, axis=1) - 1
    position = holder * CAP + order_in
    slot_table = jnp.zeros((groups * CAP,), jnp.int32).at[position].set(local_row)
    eig_table = jnp.zeros((groups * CAP, eigvec.shape[1]), jnp.float32).at[position].set(eigvec)
    got_slots = lax.all_to_all(slot_table, "group", split_axis=0, concat_axis=0, tiled=True)
    got_eig = lax.all_to_all(eig_table, "group", split_axis=0, concat_axis=0, tiled=True)
    picked = kernel_grad[got_slots]
    partial = jnp.einsum("sq,sk->qk", got_eig, picked, precision=lax.Precision.HIGHEST)
    projected = tree_psum(partial, ("blk", "group"))
    correction = jnp.dot(got_eig * eig_scale[None, :], projected, precision=lax.Precision.HIGHEST)
    return kernel_grad.at[got_slots].add(-correction)


def solution(mesh):
    in_specs = (
        P(("blk", "group"), None),
        P(("blk", "group"), None),
        P(("blk", "group"), None),
        P(("blk", "group"), None),
        P(),
        P(("blk", "group")),
    )
    out_specs = P(("blk", "group"), None)
    return jax.shard_map(body, mesh=mesh, in_specs=in_specs, out_specs=out_specs, check_vma=False)
```

```python
import jax
import jax.numpy as jnp
from jax import lax
from jax.sharding import PartitionSpec as P

D = 1024
CAP = 128


SUM_STEPS = ((3,), (0, 1, 2), (4, 5, 6))


def spread(value, bits):
    return sum(((value >> i) & 1) << b for i, b in enumerate(bits))


def tree_psum(value, axes):
    size = lax.axis_size(axes)
    me = lax.axis_index(axes)
    steps = [tuple(b for b in bits if (1 << b) < size) for bits in SUM_STEPS]
    steps = [bits for bits in steps if bits]
    current = value
    for bits in steps:
        ways = 1 << len(bits)
        mine = sum(((me >> b) & 1) << i for i, b in enumerate(bits))
        chunks = current.reshape((ways, current.shape[0] // ways) + current.shape[1:])
        total = chunks[mine]
        for d in range(1, ways):
            pairs = [(k, k ^ spread(d, bits)) for k in range(size)]
            total = total + lax.ppermute(chunks[mine ^ d], axes, pairs)
        current = total
    for bits in reversed(steps):
        ways = 1 << len(bits)
        mine = sum(((me >> b) & 1) << i for i, b in enumerate(bits))
        got = [current]
        for d in range(1, ways):
            pairs = [(k, k ^ spread(d, bits)) for k in range(size)]
            got.append(lax.ppermute(current, axes, pairs))
        stacked = jnp.stack(got)
        order = jnp.arange(ways, dtype=jnp.int32) ^ mine
        current = stacked[order].reshape((-1,) + current.shape[1:])
    return current


def body(centres, batch_x, grad, eigvec, eig_scale, sub_index):
    dims = batch_x.shape[1]
    centre_sq = jnp.sum(jnp.square(centres.astype(jnp.float32)), axis=1)
    joined = jnp.concatenate([batch_x, grad], axis=1)
    joined = lax.all_gather(joined, "group", axis=0, tiled=True)
    joined = lax.all_gather(joined, "blk", axis=0, tiled=True)
    piece_x = joined[:, :dims]
    piece_g = joined[:, dims:]
    batch_sq = jnp.sum(jnp.square(piece_x.astype(jnp.float32)), axis=1)
    inner_prod = jnp.einsum("cd,bd->cb", centres, piece_x, preferred_element_type=jnp.float32)
    distance = centre_sq[:, None] + batch_sq[None, :] - 2.0 * inner_prod
    kernel_tile = jnp.exp(-distance / (2.0 * D)).astype(jnp.bfloat16)
    kernel_grad = jnp.dot(kernel_tile, piece_g, preferred_element_type=jnp.float32)
    groups = lax.axis_size("group")
    rows_each = centres.shape[0]
    holder = sub_index // rows_each % groups
    local_row = sub_index % rows_each
    onehot = (holder[:, None] == jnp.arange(groups, dtype=jnp.int32)[None, :]).astype(jnp.int32)
    order_in = jnp.sum(jnp.cumsum(onehot, axis=0) * onehot, axis=1) - 1
    position = holder * CAP + order_in
    slot_table = jnp.zeros((groups * CAP,), jnp.int32).at[position].set(local_row)
    eig_table = jnp.zeros((groups * CAP, eigvec.shape[1]), jnp.float32).at[position].set(eigvec)
    got_slots = lax.all_to_all(slot_table, "group", split_axis=0, concat_axis=0, tiled=True)
    got_eig = lax.all_to_all(eig_table, "group", split_axis=0, concat_axis=0, tiled=True)
    picked = kernel_grad[got_slots]
    partial = jnp.einsum("sq,sk->qk", got_eig, picked, precision=lax.Precision.HIGHEST)
    projected = tree_psum(partial, ("blk", "group"))
    correction = jnp.dot(got_eig * eig_scale[None, :], projected, precision=lax.Precision.HIGHEST)
    return kernel_grad.at[got_slots].add(-correction)


def solution(mesh):
    in_specs = (
        P(("blk", "group"), None),
        P(("blk", "group"), None),
        P(("blk", "group"), None),
        P(("blk", "group"), None),
        P(),
        P(("blk", "group")),
    )
    out_specs = P(("blk", "group"), None)
    return jax.shard_map(body, mesh=mesh, in_specs=in_specs, out_specs=out_specs, check_vma=False)
```

```python
import jax
import jax.numpy as jnp
from jax import lax
from jax.sharding import PartitionSpec as P

D = 1024
CAP = 128


SUM_STEPS = ((3,), (0, 1, 2), (4, 5, 6))


def spread(value, bits):
    return sum(((value >> i) & 1) << b for i, b in enumerate(bits))


def tree_psum(value, axes):
    size = lax.axis_size(axes)
    me = lax.axis_index(axes)
    steps = [tuple(b for b in bits if (1 << b) < size) for bits in SUM_STEPS]
    steps = [bits for bits in steps if bits]
    current = value
    for bits in steps:
        ways = 1 << len(bits)
        mine = sum(((me >> b) & 1) << i for i, b in enumerate(bits))
        chunks = current.reshape((ways, current.shape[0] // ways) + current.shape[1:])
        total = chunks[mine]
        for d in range(1, ways):
            pairs = [(k, k ^ spread(d, bits)) for k in range(size)]
            total = total + lax.ppermute(chunks[mine ^ d], axes, pairs)
        current = total
    for bits in reversed(steps):
        ways = 1 << len(bits)
        mine = sum(((me >> b) & 1) << i for i, b in enumerate(bits))
        got = [current]
        for d in range(1, ways):
            pairs = [(k, k ^ spread(d, bits)) for k in range(size)]
            got.append(lax.ppermute(current, axes, pairs))
        stacked = jnp.stack(got)
        order = jnp.arange(ways, dtype=jnp.int32) ^ mine
        current = stacked[order].reshape((-1,) + current.shape[1:])
    return current


def exchange_gather(value, axis):
    size = lax.axis_size(axis)
    me = lax.axis_index(axis)
    got = [value]
    for d in range(1, size):
        got.append(lax.ppermute(value, axis, [(k, k ^ d) for k in range(size)]))
    stacked = jnp.stack(got)
    order = jnp.arange(size, dtype=jnp.int32) ^ me
    return stacked[order].reshape((-1,) + value.shape[1:])


def body(centres, batch_x, grad, eigvec, eig_scale, sub_index):
    dims = batch_x.shape[1]
    centre_sq = jnp.sum(jnp.square(centres.astype(jnp.float32)), axis=1)
    joined = jnp.concatenate([batch_x, grad], axis=1)
    joined = exchange_gather(joined, "group")
    joined = lax.all_gather(joined, "blk", axis=0, tiled=True)
    piece_x = joined[:, :dims]
    piece_g = joined[:, dims:]
    batch_sq = jnp.sum(jnp.square(piece_x.astype(jnp.float32)), axis=1)
    inner_prod = jnp.einsum("cd,bd->cb", centres, piece_x, preferred_element_type=jnp.float32)
    distance = centre_sq[:, None] + batch_sq[None, :] - 2.0 * inner_prod
    kernel_tile = jnp.exp(-distance / (2.0 * D)).astype(jnp.bfloat16)
    kernel_grad = jnp.dot(kernel_tile, piece_g, preferred_element_type=jnp.float32)
    groups = lax.axis_size("group")
    rows_each = centres.shape[0]
    holder = sub_index // rows_each % groups
    local_row = sub_index % rows_each
    onehot = (holder[:, None] == jnp.arange(groups, dtype=jnp.int32)[None, :]).astype(jnp.int32)
    order_in = jnp.sum(jnp.cumsum(onehot, axis=0) * onehot, axis=1) - 1
    position = holder * CAP + order_in
    slot_table = jnp.zeros((groups * CAP,), jnp.int32).at[position].set(local_row)
    eig_table = jnp.zeros((groups * CAP, eigvec.shape[1]), jnp.float32).at[position].set(eigvec)
    got_slots = lax.all_to_all(slot_table, "group", split_axis=0, concat_axis=0, tiled=True)
    got_eig = lax.all_to_all(eig_table, "group", split_axis=0, concat_axis=0, tiled=True)
    picked = kernel_grad[got_slots]
    partial = jnp.einsum("sq,sk->qk", got_eig, picked, precision=lax.Precision.HIGHEST)
    projected = tree_psum(partial, ("blk", "group"))
    correction = jnp.dot(got_eig * eig_scale[None, :], projected, precision=lax.Precision.HIGHEST)
    return kernel_grad.at[got_slots].add(-correction)


def solution(mesh):
    in_specs = (
        P(("blk", "group"), None),
        P(("blk", "group"), None),
        P(("blk", "group"), None),
        P(("blk", "group"), None),
        P(),
        P(("blk", "group")),
    )
    out_specs = P(("blk", "group"), None)
    return jax.shard_map(body, mesh=mesh, in_specs=in_specs, out_specs=out_specs, check_vma=False)
```

```python
import jax
import jax.numpy as jnp
from jax import lax
from jax.sharding import PartitionSpec as P

D = 1024
CAP = 128


SUM_STEPS = ((3,), (0, 1, 2), (4, 5, 6))


def spread(value, bits):
    return sum(((value >> i) & 1) << b for i, b in enumerate(bits))


def tree_psum(value, axes):
    size = lax.axis_size(axes)
    me = lax.axis_index(axes)
    steps = [tuple(b for b in bits if (1 << b) < size) for bits in SUM_STEPS]
    steps = [bits for bits in steps if bits]
    current = value
    for bits in steps:
        ways = 1 << len(bits)
        mine = sum(((me >> b) & 1) << i for i, b in enumerate(bits))
        chunks = current.reshape((ways, current.shape[0] // ways) + current.shape[1:])
        total = chunks[mine]
        for d in range(1, ways):
            pairs = [(k, k ^ spread(d, bits)) for k in range(size)]
            total = total + lax.ppermute(chunks[mine ^ d], axes, pairs)
        current = total
    for bits in reversed(steps):
        ways = 1 << len(bits)
        mine = sum(((me >> b) & 1) << i for i, b in enumerate(bits))
        got = [current]
        for d in range(1, ways):
            pairs = [(k, k ^ spread(d, bits)) for k in range(size)]
            got.append(lax.ppermute(current, axes, pairs))
        stacked = jnp.stack(got)
        order = jnp.arange(ways, dtype=jnp.int32) ^ mine
        current = stacked[order].reshape((-1,) + current.shape[1:])
    return current


def exchange_gather(value, axis):
    size = lax.axis_size(axis)
    me = lax.axis_index(axis)
    got = [value]
    for d in range(1, size):
        got.append(lax.ppermute(value, axis, [(k, k ^ d) for k in range(size)]))
    stacked = jnp.stack(got)
    order = jnp.arange(size, dtype=jnp.int32) ^ me
    return stacked[order].reshape((-1,) + value.shape[1:])


def body(centres, batch_x, grad, eigvec, eig_scale, sub_index):
    dims = batch_x.shape[1]
    centre_sq = jnp.sum(jnp.square(centres.astype(jnp.float32)), axis=1)
    joined = jnp.concatenate([batch_x, grad], axis=1)
    joined = exchange_gather(joined, "group")
    joined = lax.all_gather(joined, "blk", axis=0, tiled=True)
    piece_x = joined[:, :dims]
    piece_g = joined[:, dims:]
    batch_sq = jnp.sum(jnp.square(piece_x.astype(jnp.float32)), axis=1)
    inner_prod = jnp.einsum("cd,bd->cb", centres, piece_x, preferred_element_type=jnp.float32)
    distance = centre_sq[:, None] + batch_sq[None, :] - 2.0 * inner_prod
    kernel_tile = jnp.exp(-distance / (2.0 * D)).astype(jnp.bfloat16)
    kernel_grad = jnp.dot(kernel_tile, piece_g, preferred_element_type=jnp.float32)
    groups = lax.axis_size("group")
    rows_each = centres.shape[0]
    holder = sub_index // rows_each % groups
    local_row = sub_index % rows_each
    onehot = (holder[:, None] == jnp.arange(groups, dtype=jnp.int32)[None, :]).astype(jnp.int32)
    order_in = jnp.sum(jnp.cumsum(onehot, axis=0) * onehot, axis=1) - 1
    position = holder * CAP + order_in
    slot_table = jnp.zeros((groups * CAP,), jnp.int32).at[position].set(local_row)
    eig_table = jnp.zeros((groups * CAP, eigvec.shape[1]), jnp.float32).at[position].set(eigvec)
    got_slots = lax.all_to_all(slot_table, "group", split_axis=0, concat_axis=0, tiled=True)
    got_eig = lax.all_to_all(eig_table, "group", split_axis=0, concat_axis=0, tiled=True)
    picked = kernel_grad[got_slots]
    partial = jnp.einsum("sq,sk->qk", got_eig, picked, precision=lax.Precision.HIGHEST)
    projected = tree_psum(partial, ("blk", "group"))
    correction = jnp.dot(got_eig * eig_scale[None, :], projected, precision=lax.Precision.HIGHEST)
    upper = correction.astype(jnp.bfloat16)
    lower = (correction - upper.astype(jnp.float32)).astype(jnp.bfloat16)
    hits = (jnp.arange(rows_each, dtype=jnp.int32)[:, None] == got_slots[None, :]).astype(jnp.bfloat16)
    placed = jnp.dot(
        jnp.concatenate([hits, hits], axis=1),
        jnp.concatenate([upper, lower], axis=0),
        preferred_element_type=jnp.float32,
    )
    return kernel_grad - placed


def solution(mesh):
    in_specs = (
        P(("blk", "group"), None),
        P(("blk", "group"), None),
        P(("blk", "group"), None),
        P(("blk", "group"), None),
        P(),
        P(("blk", "group")),
    )
    out_specs = P(("blk", "group"), None)
    return jax.shard_map(body, mesh=mesh, in_specs=in_specs, out_specs=out_specs, check_vma=False)
```

```python
import jax
import jax.numpy as jnp
from jax import lax
from jax.sharding import PartitionSpec as P

D = 1024
CAP = 128


def scatter_sum(value, axis):
    size = lax.axis_size(axis)
    got = lax.all_to_all(value, axis, split_axis=0, concat_axis=0, tiled=True)
    return got.reshape((size, -1) + value.shape[1:]).sum(axis=0)


def gather_back(value, axis):
    size = lax.axis_size(axis)
    return lax.all_to_all(jnp.tile(value, (size, 1)), axis, split_axis=0, concat_axis=0, tiled=True)


def tree_psum(value):
    part = scatter_sum(scatter_sum(value, "group"), "blk")
    return gather_back(gather_back(part, "blk"), "group")


def exchange_gather(value, axis):
    size = lax.axis_size(axis)
    me = lax.axis_index(axis)
    got = [value]
    for d in range(1, size):
        got.append(lax.ppermute(value, axis, [(k, k ^ d) for k in range(size)]))
    stacked = jnp.stack(got)
    order = jnp.arange(size, dtype=jnp.int32) ^ me
    return stacked[order].reshape((-1,) + value.shape[1:])


def body(centres, batch_x, grad, eigvec, eig_scale, sub_index):
    dims = batch_x.shape[1]
    centre_sq = jnp.sum(jnp.square(centres.astype(jnp.float32)), axis=1)
    joined = jnp.concatenate([batch_x, grad], axis=1)
    joined = exchange_gather(joined, "group")
    joined = lax.all_gather(joined, "blk", axis=0, tiled=True)
    piece_x = joined[:, :dims]
    piece_g = joined[:, dims:]
    batch_sq = jnp.sum(jnp.square(piece_x.astype(jnp.float32)), axis=1)
    inner_prod = jnp.einsum("cd,bd->cb", centres, piece_x, preferred_element_type=jnp.float32)
    distance = centre_sq[:, None] + batch_sq[None, :] - 2.0 * inner_prod
    kernel_tile = jnp.exp(-distance / (2.0 * D)).astype(jnp.bfloat16)
    kernel_grad = jnp.dot(kernel_tile, piece_g, preferred_element_type=jnp.float32)
    groups = lax.axis_size("group")
    rows_each = centres.shape[0]
    holder = sub_index // rows_each % groups
    local_row = sub_index % rows_each
    onehot = (holder[:, None] == jnp.arange(groups, dtype=jnp.int32)[None, :]).astype(jnp.int32)
    order_in = jnp.sum(jnp.cumsum(onehot, axis=0) * onehot, axis=1) - 1
    position = holder * CAP + order_in
    slot_table = jnp.zeros((groups * CAP,), jnp.int32).at[position].set(local_row)
    eig_table = jnp.zeros((groups * CAP, eigvec.shape[1]), jnp.float32).at[position].set(eigvec)
    got_slots = lax.all_to_all(slot_table, "group", split_axis=0, concat_axis=0, tiled=True)
    got_eig = lax.all_to_all(eig_table, "group", split_axis=0, concat_axis=0, tiled=True)
    picked = kernel_grad[got_slots]
    partial = jnp.einsum("sq,sk->qk", got_eig, picked, precision=lax.Precision.HIGHEST)
    projected = tree_psum(partial)
    correction = jnp.dot(got_eig * eig_scale[None, :], projected, precision=lax.Precision.HIGHEST)
    rounded = lax.reduce_precision(correction, exponent_bits=8, mantissa_bits=7)
    upper = rounded.astype(jnp.bfloat16)
    lower = (correction - rounded).astype(jnp.bfloat16)
    hits = (jnp.arange(rows_each, dtype=jnp.int32)[:, None] == got_slots[None, :]).astype(jnp.bfloat16)
    placed = jnp.dot(
        jnp.concatenate([hits, hits], axis=1),
        jnp.concatenate([upper, lower], axis=0),
        preferred_element_type=jnp.float32,
    )
    return kernel_grad - placed


def solution(mesh):
    in_specs = (
        P(("blk", "group"), None),
        P(("blk", "group"), None),
        P(("blk", "group"), None),
        P(("blk", "group"), None),
        P(),
        P(("blk", "group")),
    )
    out_specs = P(("blk", "group"), None)
    return jax.shard_map(body, mesh=mesh, in_specs=in_specs, out_specs=out_specs, check_vma=False)
```

```python
import jax
import jax.numpy as jnp
from jax import lax
from jax.sharding import PartitionSpec as P

D = 1024
CAP = 128


def scatter_sum(value, axis):
    size = lax.axis_size(axis)
    got = lax.all_to_all(value, axis, split_axis=0, concat_axis=0, tiled=True)
    return got.reshape((size, -1) + value.shape[1:]).sum(axis=0)


def gather_back(value, axis):
    size = lax.axis_size(axis)
    return lax.all_to_all(jnp.tile(value, (size, 1)), axis, split_axis=0, concat_axis=0, tiled=True)


def tree_psum(value):
    part = scatter_sum(scatter_sum(value, "group"), "blk")
    return gather_back(gather_back(part, "blk"), "group")


def body(centres, batch_x, grad, eigvec, eig_scale, sub_index):
    dims = batch_x.shape[1]
    centre_sq = jnp.sum(jnp.square(centres.astype(jnp.float32)), axis=1)
    joined = jnp.concatenate([batch_x, grad], axis=1)
    joined = gather_back(joined, "group")
    joined = lax.all_gather(joined, "blk", axis=0, tiled=True)
    piece_x = joined[:, :dims]
    piece_g = joined[:, dims:]
    batch_sq = jnp.sum(jnp.square(piece_x.astype(jnp.float32)), axis=1)
    inner_prod = jnp.einsum("cd,bd->cb", centres, piece_x, preferred_element_type=jnp.float32)
    distance = centre_sq[:, None] + batch_sq[None, :] - 2.0 * inner_prod
    kernel_tile = jnp.exp(-distance / (2.0 * D)).astype(jnp.bfloat16)
    kernel_grad = jnp.dot(kernel_tile, piece_g, preferred_element_type=jnp.float32)
    groups = lax.axis_size("group")
    rows_each = centres.shape[0]
    holder = sub_index // rows_each % groups
    local_row = sub_index % rows_each
    onehot = (holder[:, None] == jnp.arange(groups, dtype=jnp.int32)[None, :]).astype(jnp.int32)
    order_in = jnp.sum(jnp.cumsum(onehot, axis=0) * onehot, axis=1) - 1
    position = holder * CAP + order_in
    slot_table = jnp.zeros((groups * CAP,), jnp.int32).at[position].set(local_row)
    eig_table = jnp.zeros((groups * CAP, eigvec.shape[1]), jnp.float32).at[position].set(eigvec)
    got_slots = lax.all_to_all(slot_table, "group", split_axis=0, concat_axis=0, tiled=True)
    got_eig = lax.all_to_all(eig_table, "group", split_axis=0, concat_axis=0, tiled=True)
    picked = kernel_grad[got_slots]
    partial = jnp.einsum("sq,sk->qk", got_eig, picked, precision=lax.Precision.HIGHEST)
    projected = tree_psum(partial)
    correction = jnp.dot(got_eig * eig_scale[None, :], projected, precision=lax.Precision.HIGHEST)
    rounded = lax.reduce_precision(correction, exponent_bits=8, mantissa_bits=7)
    upper = rounded.astype(jnp.bfloat16)
    lower = (correction - rounded).astype(jnp.bfloat16)
    hits = (jnp.arange(rows_each, dtype=jnp.int32)[:, None] == got_slots[None, :]).astype(jnp.bfloat16)
    placed = jnp.dot(
        jnp.concatenate([hits, hits], axis=1),
        jnp.concatenate([upper, lower], axis=0),
        preferred_element_type=jnp.float32,
    )
    return kernel_grad - placed


def solution(mesh):
    in_specs = (
        P(("blk", "group"), None),
        P(("blk", "group"), None),
        P(("blk", "group"), None),
        P(("blk", "group"), None),
        P(),
        P(("blk", "group")),
    )
    out_specs = P(("blk", "group"), None)
    return jax.shard_map(body, mesh=mesh, in_specs=in_specs, out_specs=out_specs, check_vma=False)
```

```python
import jax
import jax.numpy as jnp
from jax import lax
from jax.sharding import PartitionSpec as P

D = 1024
CAP = 128


def scatter_sum(value, axis):
    size = lax.axis_size(axis)
    got = lax.all_to_all(value, axis, split_axis=0, concat_axis=0, tiled=True)
    return got.reshape((size, -1) + value.shape[1:]).sum(axis=0)


def gather_back(value, axis):
    size = lax.axis_size(axis)
    return lax.all_to_all(jnp.tile(value, (size, 1)), axis, split_axis=0, concat_axis=0, tiled=True)


def tree_psum(value):
    part = scatter_sum(scatter_sum(value, "group"), "blk")
    return gather_back(gather_back(part, "blk"), "group")


def body(centres, batch_x, grad, eigvec, eig_scale, sub_index):
    dims = batch_x.shape[1]
    centre_sq = jnp.sum(jnp.square(centres.astype(jnp.float32)), axis=1)
    joined = jnp.concatenate([batch_x, grad], axis=1)
    joined = gather_back(joined, "group")
    joined = lax.all_gather(joined, "blk", axis=0, tiled=True)
    piece_x = joined[:, :dims]
    piece_g = joined[:, dims:]
    batch_sq = jnp.sum(jnp.square(piece_x.astype(jnp.float32)), axis=1)
    inner_prod = jnp.einsum("cd,bd->cb", centres, piece_x, preferred_element_type=jnp.float32)
    distance = centre_sq[:, None] + batch_sq[None, :] - 2.0 * inner_prod
    kernel_tile = jnp.exp(-distance / (2.0 * D)).astype(jnp.bfloat16)
    kernel_grad = jnp.dot(kernel_tile, piece_g, preferred_element_type=jnp.float32)
    groups = lax.axis_size("group")
    rows_each = centres.shape[0]
    holder = sub_index // rows_each % groups
    local_row = sub_index % rows_each
    onehot = (holder[:, None] == jnp.arange(groups, dtype=jnp.int32)[None, :]).astype(jnp.int32)
    order_in = jnp.sum(jnp.cumsum(onehot, axis=0) * onehot, axis=1) - 1
    position = holder * CAP + order_in
    slot_table = jnp.zeros((groups * CAP,), jnp.int32).at[position].set(local_row)
    eig_table = jnp.zeros((groups * CAP, eigvec.shape[1]), jnp.float32).at[position].set(eigvec)
    got_slots = lax.all_to_all(slot_table, "group", split_axis=0, concat_axis=0, tiled=True)
    got_eig = lax.all_to_all(eig_table, "group", split_axis=0, concat_axis=0, tiled=True)
    sub_rows = centres[got_slots]
    sub_inner = jnp.einsum("cd,bd->cb", sub_rows, piece_x, preferred_element_type=jnp.float32)
    sub_distance = centre_sq[got_slots][:, None] + batch_sq[None, :] - 2.0 * sub_inner
    sub_tile = jnp.exp(-sub_distance / (2.0 * D)).astype(jnp.bfloat16)
    picked = jnp.dot(sub_tile, piece_g, preferred_element_type=jnp.float32)
    partial = jnp.einsum("sq,sk->qk", got_eig, picked, precision=lax.Precision.HIGHEST)
    projected = tree_psum(partial)
    correction = jnp.dot(got_eig * eig_scale[None, :], projected, precision=lax.Precision.HIGHEST)
    rounded = lax.reduce_precision(correction, exponent_bits=8, mantissa_bits=7)
    upper = rounded.astype(jnp.bfloat16)
    lower = (correction - rounded).astype(jnp.bfloat16)
    hits = (jnp.arange(rows_each, dtype=jnp.int32)[:, None] == got_slots[None, :]).astype(jnp.bfloat16)
    placed = jnp.dot(
        jnp.concatenate([hits, hits], axis=1),
        jnp.concatenate([upper, lower], axis=0),
        preferred_element_type=jnp.float32,
    )
    return kernel_grad - placed


def solution(mesh):
    in_specs = (
        P(("blk", "group"), None),
        P(("blk", "group"), None),
        P(("blk", "group"), None),
        P(("blk", "group"), None),
        P(),
        P(("blk", "group")),
    )
    out_specs = P(("blk", "group"), None)
    return jax.shard_map(body, mesh=mesh, in_specs=in_specs, out_specs=out_specs, check_vma=False)
```

```python
import jax
import jax.numpy as jnp
from jax import lax
from jax.sharding import PartitionSpec as P

D = 1024
CAP = 128


def scatter_sum(value, axis):
    size = lax.axis_size(axis)
    got = lax.all_to_all(value, axis, split_axis=0, concat_axis=0, tiled=True)
    return got.reshape((size, -1) + value.shape[1:]).sum(axis=0)


def gather_back(value, axis):
    size = lax.axis_size(axis)
    return lax.all_to_all(jnp.tile(value, (size, 1)), axis, split_axis=0, concat_axis=0, tiled=True)


def tree_psum(value):
    part = scatter_sum(scatter_sum(value, "group"), "blk")
    return gather_back(gather_back(part, "blk"), "group")


def body(centres, batch_x, grad, eigvec, eig_scale, sub_index):
    dims = batch_x.shape[1]
    centre_sq = jnp.sum(jnp.square(centres.astype(jnp.float32)), axis=1)
    joined = jnp.concatenate([batch_x, grad], axis=1)
    joined = gather_back(joined, "group")
    joined = lax.all_gather(joined, "blk", axis=0, tiled=True)
    piece_x = joined[:, :dims]
    piece_g = joined[:, dims:]
    batch_sq = jnp.sum(jnp.square(piece_x.astype(jnp.float32)), axis=1)
    inner_prod = jnp.einsum("cd,bd->cb", centres, piece_x, preferred_element_type=jnp.float32)
    distance = centre_sq[:, None] + batch_sq[None, :] - 2.0 * inner_prod
    kernel_tile = jnp.exp(-distance / (2.0 * D)).astype(jnp.bfloat16)
    kernel_grad = jnp.dot(kernel_tile, piece_g, preferred_element_type=jnp.float32)
    groups = lax.axis_size("group")
    rows_each = centres.shape[0]
    holder = sub_index // rows_each % groups
    local_row = sub_index % rows_each
    onehot = (holder[:, None] == jnp.arange(groups, dtype=jnp.int32)[None, :]).astype(jnp.int32)
    order_in = jnp.sum(jnp.cumsum(onehot, axis=0) * onehot, axis=1) - 1
    position = holder * CAP + order_in
    slot_table = jnp.zeros((groups * CAP,), jnp.int32).at[position].set(local_row)
    eig_table = jnp.zeros((groups * CAP, eigvec.shape[1]), jnp.float32).at[position].set(eigvec)
    got_slots = lax.all_to_all(slot_table, "group", split_axis=0, concat_axis=0, tiled=True)
    got_eig = lax.all_to_all(eig_table, "group", split_axis=0, concat_axis=0, tiled=True)
    sub_rows = centres[got_slots]
    sub_inner = jnp.einsum("cd,bd->cb", sub_rows, piece_x, preferred_element_type=jnp.float32)
    sub_distance = centre_sq[got_slots][:, None] + batch_sq[None, :] - 2.0 * sub_inner
    sub_tile = jnp.exp(-sub_distance / (2.0 * D)).astype(jnp.bfloat16)
    picked = jnp.dot(sub_tile, piece_g, preferred_element_type=jnp.float32)
    partial = jnp.einsum("sq,sk->qk", got_eig, picked, precision=lax.Precision.HIGH)
    projected = tree_psum(partial)
    correction = jnp.dot(got_eig * eig_scale[None, :], projected, precision=lax.Precision.HIGH)
    rounded = lax.reduce_precision(correction, exponent_bits=8, mantissa_bits=7)
    upper = rounded.astype(jnp.bfloat16)
    lower = (correction - rounded).astype(jnp.bfloat16)
    hits = (jnp.arange(rows_each, dtype=jnp.int32)[:, None] == got_slots[None, :]).astype(jnp.bfloat16)
    placed = jnp.dot(
        jnp.concatenate([hits, hits], axis=1),
        jnp.concatenate([upper, lower], axis=0),
        preferred_element_type=jnp.float32,
    )
    return kernel_grad - placed


def solution(mesh):
    in_specs = (
        P(("blk", "group"), None),
        P(("blk", "group"), None),
        P(("blk", "group"), None),
        P(("blk", "group"), None),
        P(),
        P(("blk", "group")),
    )
    out_specs = P(("blk", "group"), None)
    return jax.shard_map(body, mesh=mesh, in_specs=in_specs, out_specs=out_specs, check_vma=False)
```

```python
import jax
import jax.numpy as jnp
from jax import lax
from jax.sharding import PartitionSpec as P

D = 1024
CAP = 128


def scatter_sum(value, axis):
    size = lax.axis_size(axis)
    got = lax.all_to_all(value, axis, split_axis=0, concat_axis=0, tiled=True)
    return got.reshape((size, -1) + value.shape[1:]).sum(axis=0)


def gather_back(value, axis):
    size = lax.axis_size(axis)
    return lax.all_to_all(jnp.tile(value, (size, 1)), axis, split_axis=0, concat_axis=0, tiled=True)


def tree_psum(value):
    part = scatter_sum(scatter_sum(value, "group"), "blk")
    return gather_back(gather_back(part, "blk"), "group")


def body(centres, batch_x, grad, eigvec, eig_scale, sub_index):
    dims = batch_x.shape[1]
    centre_sq = jnp.sum(jnp.square(centres.astype(jnp.float32)), axis=1)
    joined = jnp.concatenate([batch_x, grad], axis=1)
    joined = gather_back(joined, "group")
    joined = lax.all_gather(joined, "blk", axis=0, tiled=True)
    piece_x = joined[:, :dims]
    piece_g = joined[:, dims:]
    batch_sq = jnp.sum(jnp.square(piece_x.astype(jnp.float32)), axis=1)
    inner_prod = jnp.einsum("cd,bd->cb", centres, piece_x, preferred_element_type=jnp.float32)
    distance = centre_sq[:, None] + batch_sq[None, :] - 2.0 * inner_prod
    kernel_tile = jnp.exp(-distance / (2.0 * D)).astype(jnp.bfloat16)
    kernel_grad = lax.optimization_barrier(
        jnp.dot(kernel_tile, piece_g, preferred_element_type=jnp.float32)
    )
    groups = lax.axis_size("group")
    rows_each = centres.shape[0]
    holder = sub_index // rows_each % groups
    local_row = sub_index % rows_each
    onehot = (holder[:, None] == jnp.arange(groups, dtype=jnp.int32)[None, :]).astype(jnp.int32)
    order_in = jnp.sum(jnp.cumsum(onehot, axis=0) * onehot, axis=1) - 1
    position = holder * CAP + order_in
    slot_table = jnp.zeros((groups * CAP,), jnp.int32).at[position].set(local_row)
    eig_table = jnp.zeros((groups * CAP, eigvec.shape[1]), jnp.float32).at[position].set(eigvec)
    got_slots = lax.all_to_all(slot_table, "group", split_axis=0, concat_axis=0, tiled=True)
    got_eig = lax.all_to_all(eig_table, "group", split_axis=0, concat_axis=0, tiled=True)
    sub_rows = centres[got_slots]
    sub_inner = jnp.einsum("cd,bd->cb", sub_rows, piece_x, preferred_element_type=jnp.float32)
    sub_distance = centre_sq[got_slots][:, None] + batch_sq[None, :] - 2.0 * sub_inner
    sub_tile = jnp.exp(-sub_distance / (2.0 * D)).astype(jnp.bfloat16)
    picked = jnp.dot(sub_tile, piece_g, preferred_element_type=jnp.float32)
    partial = jnp.einsum("sq,sk->qk", got_eig, picked, precision=lax.Precision.HIGH)
    projected = tree_psum(partial)
    correction = jnp.dot(got_eig * eig_scale[None, :], projected, precision=lax.Precision.HIGH)
    rounded = lax.reduce_precision(correction, exponent_bits=8, mantissa_bits=7)
    upper = rounded.astype(jnp.bfloat16)
    lower = (correction - rounded).astype(jnp.bfloat16)
    hits = (jnp.arange(rows_each, dtype=jnp.int32)[:, None] == got_slots[None, :]).astype(jnp.bfloat16)
    placed = jnp.dot(
        jnp.concatenate([hits, hits], axis=1),
        jnp.concatenate([upper, lower], axis=0),
        preferred_element_type=jnp.float32,
    )
    return kernel_grad - placed


def solution(mesh):
    in_specs = (
        P(("blk", "group"), None),
        P(("blk", "group"), None),
        P(("blk", "group"), None),
        P(("blk", "group"), None),
        P(),
        P(("blk", "group")),
    )
    out_specs = P(("blk", "group"), None)
    return jax.shard_map(body, mesh=mesh, in_specs=in_specs, out_specs=out_specs, check_vma=False)
```

```python
import jax
import jax.numpy as jnp
from jax import lax
from jax.sharding import PartitionSpec as P

D = 1024
CAP = 128


def scatter_sum(value, axis):
    size = lax.axis_size(axis)
    got = lax.all_to_all(value, axis, split_axis=0, concat_axis=0, tiled=True)
    return got.reshape((size, -1) + value.shape[1:]).sum(axis=0)


def gather_back(value, axis):
    size = lax.axis_size(axis)
    return lax.all_to_all(jnp.tile(value, (size, 1)), axis, split_axis=0, concat_axis=0, tiled=True)


def tree_psum(value):
    part = scatter_sum(scatter_sum(value, "group"), "blk")
    return gather_back(gather_back(part, "blk"), "group")


def body(centres, batch_x, grad, eigvec, eig_scale, sub_index):
    dims = batch_x.shape[1]
    centre_sq = jnp.sum(jnp.square(centres.astype(jnp.float32)), axis=1)
    joined = jnp.concatenate([batch_x, grad], axis=1)
    joined = gather_back(joined, "group")
    joined = lax.all_gather(joined, "blk", axis=0, tiled=True)
    piece_x = joined[:, :dims]
    piece_g = joined[:, dims:]
    batch_sq = jnp.sum(jnp.square(piece_x.astype(jnp.float32)), axis=1)
    halves = []
    half = centres.shape[0] // 2
    for lo in (0, half):
        block = centres[lo : lo + half]
        inner_prod = jnp.einsum("cd,bd->cb", block, piece_x, preferred_element_type=jnp.float32)
        distance = centre_sq[lo : lo + half][:, None] + batch_sq[None, :] - 2.0 * inner_prod
        kernel_tile = jnp.exp(-distance / (2.0 * D)).astype(jnp.bfloat16)
        halves.append(
            lax.optimization_barrier(jnp.dot(kernel_tile, piece_g, preferred_element_type=jnp.float32))
        )
    kernel_grad = jnp.concatenate(halves, axis=0)
    groups = lax.axis_size("group")
    rows_each = centres.shape[0]
    holder = sub_index // rows_each % groups
    local_row = sub_index % rows_each
    onehot = (holder[:, None] == jnp.arange(groups, dtype=jnp.int32)[None, :]).astype(jnp.int32)
    order_in = jnp.sum(jnp.cumsum(onehot, axis=0) * onehot, axis=1) - 1
    position = holder * CAP + order_in
    slot_table = jnp.zeros((groups * CAP,), jnp.int32).at[position].set(local_row)
    eig_table = jnp.zeros((groups * CAP, eigvec.shape[1]), jnp.float32).at[position].set(eigvec)
    got_slots = lax.all_to_all(slot_table, "group", split_axis=0, concat_axis=0, tiled=True)
    got_eig = lax.all_to_all(eig_table, "group", split_axis=0, concat_axis=0, tiled=True)
    sub_rows = centres[got_slots]
    sub_inner = jnp.einsum("cd,bd->cb", sub_rows, piece_x, preferred_element_type=jnp.float32)
    sub_distance = centre_sq[got_slots][:, None] + batch_sq[None, :] - 2.0 * sub_inner
    sub_tile = jnp.exp(-sub_distance / (2.0 * D)).astype(jnp.bfloat16)
    picked = jnp.dot(sub_tile, piece_g, preferred_element_type=jnp.float32)
    partial = jnp.einsum("sq,sk->qk", got_eig, picked, precision=lax.Precision.HIGH)
    projected = tree_psum(partial)
    correction = jnp.dot(got_eig * eig_scale[None, :], projected, precision=lax.Precision.HIGH)
    rounded = lax.reduce_precision(correction, exponent_bits=8, mantissa_bits=7)
    upper = rounded.astype(jnp.bfloat16)
    lower = (correction - rounded).astype(jnp.bfloat16)
    hits = (jnp.arange(rows_each, dtype=jnp.int32)[:, None] == got_slots[None, :]).astype(jnp.bfloat16)
    placed = jnp.dot(
        jnp.concatenate([hits, hits], axis=1),
        jnp.concatenate([upper, lower], axis=0),
        preferred_element_type=jnp.float32,
    )
    return kernel_grad - placed


def solution(mesh):
    in_specs = (
        P(("blk", "group"), None),
        P(("blk", "group"), None),
        P(("blk", "group"), None),
        P(("blk", "group"), None),
        P(),
        P(("blk", "group")),
    )
    out_specs = P(("blk", "group"), None)
    return jax.shard_map(body, mesh=mesh, in_specs=in_specs, out_specs=out_specs, check_vma=False)
```
